128 devices in a mesh: px: 8 (over x, core), py: 16 (over z, y).
Axes of the slice: x: 4, y: 4, z: 4, core: 2. Of those that a mesh axis runs over, the one named last changes fastest.
Arguments:
- displacement: float32 [6, 128, 2048], P(None, 'px', 'py'), may hold values from -4 to 4
- velocity: float32 [6, 128, 2048], P(None, 'px', 'py'), may hold values from -6 to 6
- load: float32 [6, 128, 2048], P(None, 'px', 'py'), may hold values from -24 to 24
- inv_mass: float32 [6, 128, 2048], P(None, 'px', 'py'), may hold values from 0.2 to 1
- history: float32 [128, 128, 2048], P(None, 'px', 'py'), may hold values from -6 to 6
- contact_home: float32 [128, 128, 2048], P(None, 'px', 'py'), may hold values from 0.25 to 4
- recv_contact: float32 [8, 16, 128, 1152], P('px', 'py'), may hold values from 0.25 to 4
- stiff_base: float32 [24, 24], replicated, as said below
- strain_map: float32 [128, 24], replicated, may hold values from -1.25 to 1.25
- slot_table: int32 [8, 16, 1152], P('px', 'py'), may hold values from 0 to 2048, as said below
Outputs:
- springback: float32 [6, 128, 2048], P(None, 'px', 'py')
- velocity_out: float32 [6, 128, 2048], P(None, 'px', 'py')
- history_out: float32 [128, 128, 2048], P(None, 'px', 'py')
- residual: float32 [6, 128, 2048], P(None, 'px', 'py')
The draws below stay inside these ranges and needn't reach their ends.
Inputs may be any that keep to these rules, and one draw needn't show every extreme that they name: `slot_table`: for each source block and destination device d, the slots d * 9 .. d * 9 + 8 hold distinct local shell indices first and then 16 * 128; no shell appears twice in one source block; no block sends to itself; every source block fills all 9 slots toward some destination, and about half of the source blocks fill all slots toward every other device. `stiff_base`: Symmetric, with diagonal entries of 5 to 7 and off-diagonal entries of magnitude at most 0.2.
All inputs are finite; a program needn't handle non-finite values.
Results may differ from the reference program's by a relative error of at most 0.0003.
Values sent between devices are 32-bit elements; how exact they have to be, the bound alone decides.
No kernel may reach another device: no remote copies, remote signals or barrier semaphores. Data moves between devices by JAX's collectives and lax.ppermute only.
A program may use at most 128 MiB of HBM per device.

```python
import math
import jax
import jax.numpy as jnp
from jax import lax

CX = 16
CY = 128
HIST = 128
ITERS = 2
CAP = 9
NX = 128
NY = 2048
N_PX = 8
N_PY = 16


def draw_stiff_base(key, part):
    off = jax.random.uniform(key, (24, 24), jnp.float32, -0.1, 0.1)
    sym = off + off.T
    diag = jax.random.uniform(jax.random.fold_in(key, 1), (24,), jnp.float32, 5.0, 7.0)
    eye = jnp.eye(24, dtype=jnp.float32)
    return sym * (1.0 - eye) + eye * diag[None, :]


def draw_slot_table(key, part):
    devices = N_PX * N_PY
    cells = CX * CY

    def one(source):
        inner = jax.random.fold_in(key, source)
        counts = jax.random.randint(jax.random.fold_in(inner, 1), (devices,), 0, CAP + 1)
        heavy = jax.random.randint(jax.random.fold_in(inner, 3), (), 0, 2)
        counts = jnp.where(heavy == 1, CAP, counts)
        dest = jnp.arange(devices)
        counts = jnp.where(dest == (source + 1) % devices, CAP, counts)
        counts = jnp.where(dest == source, 0, counts)
        start = jnp.cumsum(counts) - counts
        order = jax.random.permutation(jax.random.fold_in(inner, 2), cells)
        slot = jnp.arange(CAP)
        position = start[:, None] + slot[None, :]
        live = slot[None, :] < counts[:, None]
        picked = order[jnp.minimum(position, cells - 1)]
        return jnp.where(live, picked, cells).reshape(-1).astype(jnp.int32)
    table = jax.vmap(one)(jnp.arange(devices))
    return table.reshape(N_PX, N_PY, devices * CAP)


def levels(own_key, dims, shards, smallest, high):
    def one(dim, shards_of):
        draws = jax.random.uniform(jax.random.fold_in(jax.random.fold_in(own_key, 6), dim), (shards_of,), jnp.float32, smallest / len(shards), high / len(shards))
        return jnp.repeat(jnp.exp(draws), dims[dim] // shards_of).reshape((-1,) + (1,) * (len(dims) - dim - 1))

    gain = one(*shards[0])
    for cut in shards[1:]:
        gain = gain * one(*cut)
    return gain


def scatter_about(key, extent, spread, reach, pieces=(), kind=jnp.bfloat16):
    values = spread * jax.random.normal(key, extent, jnp.float32)
    if pieces:
        values = values * levels(key, extent, pieces, -0.22, 0.18)
    return jnp.clip(values, -reach, reach).astype(kind)


def setup_inputs(seed: int = 0) -> dict:
    key_of = jax.random.split(jax.random.key(seed), 11)
    displacement = scatter_about(key_of[0], (6, NX, NY), 0.5, 4.0, ((1, 8), (2, 16)), jnp.float32)
    velocity = scatter_about(key_of[1], (6, NX, NY), 1.0, 6.0, ((1, 8), (2, 16)), jnp.float32)
    load = scatter_about(key_of[2], (6, NX, NY), 4.0, 24.0, ((1, 8), (2, 16)), jnp.float32)
    inv_mass = jnp.clip(jnp.exp(math.log(1.0) - 1.609438 * jax.random.uniform(key_of[3], (6, NX, NY), jnp.float32) ** levels(key_of[3], (6, NX, NY), ((1, 8), (2, 16)), -0.2, 0.2)), 0.2, 1.0)
    history = scatter_about(key_of[4], (HIST, NX, NY), 1.0, 6.0, ((1, 8), (2, 16)), jnp.float32)
    contact_home = jnp.clip(jnp.exp(math.log(4.0) - 2.7725887 * jax.random.uniform(key_of[5], (HIST, NX, NY), jnp.float32) ** levels(key_of[5], (HIST, NX, NY), ((1, 8), (2, 16)), -0.2, 0.2)), 0.25, 4.0)
    recv_contact = jnp.clip(jnp.exp(math.log(4.0) - 2.7725887 * jax.random.uniform(key_of[6], (N_PX, N_PY, HIST, N_PX * N_PY * CAP), jnp.float32) ** levels(key_of[6], (N_PX, N_PY, HIST, N_PX * N_PY * CAP), ((0, 8), (1, 16)), -0.2, 0.2)), 0.25, 4.0)
    stiff_base = draw_stiff_base(jax.random.fold_in(key_of[10], 71), 0)
    strain_map = scatter_about(key_of[8], (HIST, 24), 24 ** -0.5, 1.25, (), jnp.float32)
    slot_table = draw_slot_table(jax.random.fold_in(key_of[10], 71), 0)
    return {"displacement": displacement, "velocity": velocity, "load": load, "inv_mass": inv_mass, "history": history, "contact_home": contact_home, "recv_contact": recv_contact, "stiff_base": stiff_base, "strain_map": strain_map, "slot_table": slot_table}


HIGH = lax.Precision.HIGHEST
STEP = 0.2
CORNERS = ((0, 0), (1, 0), (0, 1), (1, 1))


def gather_corners(field):
    rows, cols = field.shape[1], field.shape[2]
    padded = jnp.pad(field, ((0, 0), (0, 1), (0, 1)))
    return jnp.concatenate([padded[:, dx:dx + rows, dy:dy + cols] for dx, dy in CORNERS], axis=0)


def scatter_corners(forces):
    rows, cols = forces.shape[1], forces.shape[2]
    padded = jnp.pad(forces, ((0, 0), (1, 0), (1, 0)))
    total = jnp.zeros((6, rows, cols), jnp.float32)
    for index, (dx, dy) in enumerate(CORNERS):
        total = total + padded[6 * index:6 * index + 6, 1 - dx:1 - dx + rows, 1 - dy:1 - dy + cols]
    return total


def to_blocks(field):
    chans = field.shape[0]
    split = field.reshape(chans, N_PX, CX, N_PY, CY).transpose(1, 3, 0, 2, 4)
    return split.reshape(N_PX * N_PY, chans, CX * CY)


def from_blocks(blocks):
    chans = blocks.shape[1]
    split = blocks.reshape(N_PX, N_PY, chans, CX, CY).transpose(2, 0, 3, 1, 4)
    return split.reshape(chans, N_PX * CX, N_PY * CY)


def reference(displacement, velocity, load, inv_mass, history, contact_home, recv_contact, stiff_base, strain_map, slot_table):
    force_start = scatter_corners(jnp.einsum("ab,bxy->axy", stiff_base, gather_corners(displacement), precision=HIGH))
    velocity_out = velocity + STEP * inv_mass * (load - force_start)
    moved = displacement + STEP * velocity_out
    hist = history.shape[0]
    shells = gather_corners(displacement).reshape(24, -1)
    history_out = history + jnp.dot(strain_map, shells, precision=HIGH).reshape(history.shape)
    devices = N_PX * N_PY
    held = recv_contact.reshape(devices, hist, devices, CAP).transpose(2, 1, 0, 3).reshape(devices, hist, devices * CAP)
    targets = slot_table.reshape(devices, devices * CAP).astype(jnp.int32)
    placed = jax.vmap(lambda block, index, values: block.at[:, index].set(values, mode="drop"))(to_blocks(contact_home), targets, held)
    contact = from_blocks(placed)
    pairs = (strain_map[:, :, None] * strain_map[:, None, :]).reshape(hist, 576)
    weights = (jax.nn.softplus(history_out) * contact).reshape(hist, -1)
    tangent = stiff_base.reshape(576, 1) + jnp.dot(pairs.T, weights, precision=HIGH)
    tangent = tangent.reshape((24, 24) + history.shape[1:])

    def operate(field):
        return scatter_corners(jnp.einsum("abxy,bxy->axy", tangent, gather_corners(field), precision=HIGH))

    rhs = load - force_start
    solution = jnp.zeros_like(rhs)
    residual = rhs
    direction = rhs
    norm_now = jnp.sum(residual * residual)
    for step in range(ITERS):
        image = operate(direction)
        alpha = norm_now / jnp.sum(direction * image)
        solution = solution + alpha * direction
        residual = residual - alpha * image
        if step + 1 < ITERS:
            norm_next = jnp.sum(residual * residual)
            direction = residual + (norm_next / norm_now) * direction
            norm_now = norm_next
    return (moved + solution, velocity_out, history_out, residual)
```

```python
import jax
import jax.numpy as jnp
from jax import lax
from jax.sharding import PartitionSpec as P

ITERS = 2


HIGH = lax.Precision.HIGHEST
STEP = 0.2
CORNERS = ((0, 0), (1, 0), (0, 1), (1, 1))


def with_halo(shard, sides, width):
    for axis, dim in sides:
        devices, length = (lax.axis_size(axis), shard.shape[dim])
        up = [(i, (i + 1) % devices) for i in range(devices - 1)]
        down = [(j, i) for i, j in up]
        last = lax.slice_in_dim(shard, length - width, length, axis=dim)
        leading = lax.slice_in_dim(shard, 0, width, axis=dim)
        before = lax.ppermute(last, axis, up)
        after = lax.ppermute(leading, axis, down)
        shard = jnp.concatenate([before, shard, after], axis=dim)
    return shard


def shifted(shard, axis, by):
    devices = lax.axis_size(axis)
    pairs = [(i, i + by) for i in range(devices) if 0 <= i + by < devices]
    return lax.ppermute(shard, axis, pairs)


def all_sum(value):
    for axis in ("px", "py"):
        devices = lax.axis_size(axis)
        stride = 1
        while stride < devices:
            radix = min(4, devices // stride)
            total = value
            for k in range(1, radix):
                pairs = []
                for i in range(devices):
                    digit = (i // stride) % radix
                    pairs.append((i, i + (((digit + k) % radix) - digit) * stride))
                total = total + lax.ppermute(value, axis, pairs)
            value = total
            stride *= radix
    return value


def gather_shells(field):
    rows, cols = (field.shape[1] - 2, field.shape[2] - 2)
    return jnp.concatenate(
        [field[:, dx : dx + rows + 1, dy : dy + cols + 1] for dx, dy in CORNERS], axis=0
    )


def scatter_nodes(forces):
    rows, cols = (forces.shape[1] - 1, forces.shape[2] - 1)
    row_keep = (jnp.arange(rows + 1) > 0) | (lax.axis_index("px") > 0)
    col_keep = (jnp.arange(cols + 1) > 0) | (lax.axis_index("py") > 0)
    keep = (row_keep[:, None] & col_keep[None, :]).astype(jnp.float32)
    forces = forces * keep[None, :, :]
    total = jnp.zeros((6, rows, cols), jnp.float32)
    for index, (dx, dy) in enumerate(CORNERS):
        total = (
            total
            + forces[6 * index : 6 * index + 6, 1 - dx : 1 - dx + rows, 1 - dy : 1 - dy + cols]
        )
    return total


def shards(
    displacement,
    velocity,
    load,
    inv_mass,
    history,
    contact_home,
    recv_contact,
    stiff_base,
    strain_map,
    slot_table,
):
    hist = history.shape[0]
    rows, cols = (displacement.shape[1], displacement.shape[2])
    cells = rows * cols

    targets = slot_table.reshape(-1)
    devices = lax.axis_size("px") * lax.axis_size("py")
    width = targets.shape[0] // devices
    held = recv_contact.reshape(hist, devices, width)
    arrived = lax.all_to_all(held, ("px", "py"), split_axis=1, concat_axis=1, tiled=True)

    def with_base(shells):
        return jnp.einsum("ab,bxy->axy", stiff_base, shells, precision=HIGH)

    start_shells = gather_shells(with_halo(displacement, (("px", 1), ("py", 2)), 1))
    force_start = scatter_nodes(with_base(start_shells))
    velocity_out = velocity + STEP * inv_mass * (load - force_start)
    moved = displacement + STEP * velocity_out
    own = start_shells[:, 1:, 1:].reshape(24, cells)
    history_new = history.reshape(hist, cells) + jnp.dot(strain_map, own, precision=HIGH)

    contact = (
        contact_home.reshape(hist, cells)
        .at[:, targets]
        .set(arrived.reshape(hist, devices * width), mode="drop")
    )
    weights = (jax.nn.softplus(history_new) * contact).reshape(hist, rows, cols)
    lower_row = shifted(weights[:, -1:, :], "px", 1)
    tall = jnp.concatenate([lower_row, weights], axis=1)
    lower_col = shifted(tall[:, :, -1:], "py", 1)
    extended = jnp.concatenate([lower_col, tall], axis=2)

    def operate(field):
        shells = gather_shells(with_halo(field, (("px", 1), ("py", 2)), 1))
        strains = jnp.einsum("hb,bxy->hxy", strain_map, shells, precision=HIGH)
        forces = jnp.einsum("hb,hxy->bxy", strain_map, extended * strains, precision=HIGH)
        return scatter_nodes(forces + with_base(shells))

    rhs = load - force_start
    solution = jnp.zeros_like(rhs)
    residual = rhs
    direction = rhs
    norm_now = all_sum(jnp.sum(residual * residual).reshape(1))[0]
    for step in range(ITERS):
        image = operate(direction)
        alpha = norm_now / all_sum(jnp.sum(direction * image).reshape(1))[0]
        solution = solution + alpha * direction
        residual = residual - alpha * image
        if step + 1 < ITERS:
            norm_next = all_sum(jnp.sum(residual * residual).reshape(1))[0]
            direction = residual + norm_next / norm_now * direction
            norm_now = norm_next
    return (moved + solution, velocity_out, history_new.reshape(hist, rows, cols), residual)


def solution(mesh):
    return jax.shard_map(
        shards,
        mesh=mesh,
        in_specs=(
            P(None, "px", "py"),
            P(None, "px", "py"),
            P(None, "px", "py"),
            P(None, "px", "py"),
            P(None, "px", "py"),
            P(None, "px", "py"),
            P("px", "py", None, None),
            P(),
            P(),
            P("px", "py", None),
        ),
        out_specs=(
            P(None, "px", "py"),
            P(None, "px", "py"),
            P(None, "px", "py"),
            P(None, "px", "py"),
        ),
        check_vma=False,
    )
```

```python
import jax
import jax.numpy as jnp
from jax import lax
from jax.sharding import PartitionSpec as P

ITERS = 2


HIGH = lax.Precision.HIGHEST
STEP = 0.2
CORNERS = ((0, 0), (1, 0), (0, 1), (1, 1))


def with_halo(shard, sides, width):
    for axis, dim in sides:
        devices, length = (lax.axis_size(axis), shard.shape[dim])
        up = [(i, (i + 1) % devices) for i in range(devices - 1)]
        down = [(j, i) for i, j in up]
        last = lax.slice_in_dim(shard, length - width, length, axis=dim)
        leading = lax.slice_in_dim(shard, 0, width, axis=dim)
        before = lax.ppermute(last, axis, up)
        after = lax.ppermute(leading, axis, down)
        shard = jnp.concatenate([before, shard, after], axis=dim)
    return shard


def shifted(shard, axis, by):
    devices = lax.axis_size(axis)
    pairs = [(i, i + by) for i in range(devices) if 0 <= i + by < devices]
    return lax.ppermute(shard, axis, pairs)


def all_sum(value):
    for axis in ("px", "py"):
        devices = lax.axis_size(axis)
        stride = 1
        while stride < devices:
            radix = min(4, devices // stride)
            total = value
            for k in range(1, radix):
                pairs = []
                for i in range(devices):
                    digit = (i // stride) % radix
                    pairs.append((i, i + (((digit + k) % radix) - digit) * stride))
                total = total + lax.ppermute(value, axis, pairs)
            value = total
            stride *= radix
    return value


def gather_shells(field):
    rows, cols = (field.shape[1] - 2, field.shape[2] - 2)
    return jnp.concatenate(
        [field[:, dx : dx + rows + 1, dy : dy + cols + 1] for dx, dy in CORNERS], axis=0
    )


def scatter_nodes(forces):
    rows, cols = (forces.shape[1] - 1, forces.shape[2] - 1)
    row_keep = (jnp.arange(rows + 1) > 0) | (lax.axis_index("px") > 0)
    col_keep = (jnp.arange(cols + 1) > 0) | (lax.axis_index("py") > 0)
    keep = (row_keep[:, None] & col_keep[None, :]).astype(jnp.float32)
    forces = forces * keep[None, :, :]
    total = jnp.zeros((6, rows, cols), jnp.float32)
    for index, (dx, dy) in enumerate(CORNERS):
        total = (
            total
            + forces[6 * index : 6 * index + 6, 1 - dx : 1 - dx + rows, 1 - dy : 1 - dy + cols]
        )
    return total


def shards(
    displacement,
    velocity,
    load,
    inv_mass,
    history,
    contact_home,
    recv_contact,
    stiff_base,
    strain_map,
    slot_table,
):
    hist = history.shape[0]
    rows, cols = (displacement.shape[1], displacement.shape[2])
    cells = rows * cols

    targets = slot_table.reshape(-1)
    devices = lax.axis_size("px") * lax.axis_size("py")
    width = targets.shape[0] // devices
    held = recv_contact.reshape(hist, devices, width)
    arrived = lax.all_to_all(held, ("px", "py"), split_axis=1, concat_axis=1, tiled=True)

    def with_base(shells):
        return jnp.einsum("ab,bxy->axy", stiff_base, shells, precision=HIGH)

    start_shells = gather_shells(with_halo(displacement, (("px", 1), ("py", 2)), 1))
    force_start = scatter_nodes(with_base(start_shells))
    velocity_out = velocity + STEP * inv_mass * (load - force_start)
    moved = displacement + STEP * velocity_out
    own = start_shells[:, 1:, 1:].reshape(24, cells)
    history_new = history.reshape(hist, cells) + jnp.dot(strain_map, own, precision=HIGH)

    contact = (
        contact_home.reshape(hist, cells)
        .at[:, targets]
        .set(arrived.reshape(hist, devices * width), mode="drop")
    )
    weights = (jax.nn.softplus(history_new) * contact).reshape(hist, rows, cols)
    lower_row = shifted(weights[:, -1:, :], "px", 1)
    tall = jnp.concatenate([lower_row, weights], axis=1)
    lower_col = shifted(tall[:, :, -1:], "py", 1)
    extended = jnp.concatenate([lower_col, tall], axis=2)

    def operate(field):
        shells = gather_shells(with_halo(field, (("px", 1), ("py", 2)), 1))
        strains = jnp.einsum("hb,bxy->hxy", strain_map, shells, precision=HIGH)
        forces = jnp.einsum("hb,hxy->bxy", strain_map, extended * strains, precision=HIGH)
        return scatter_nodes(forces + with_base(shells))

    rhs = load - force_start
    image = operate(rhs)
    again = operate(image)
    first = all_sum(jnp.stack([jnp.sum(rhs * rhs), jnp.sum(rhs * image)]))
    norm_now, curvature = first[0], first[1]
    alpha = norm_now / curvature
    residual = rhs - alpha * image
    bent = image - alpha * again
    second = all_sum(
        jnp.stack(
            [
                jnp.sum(residual * residual),
                jnp.sum(residual * bent),
                jnp.sum(residual * image),
                jnp.sum(rhs * bent),
            ]
        )
    )
    norm_next = second[0]
    beta = norm_next / norm_now
    direction = residual + beta * rhs
    turned = bent + beta * image
    curvature_next = second[1] + beta * (second[2] + second[3]) + beta * beta * curvature
    alpha_next = norm_next / curvature_next
    solution = alpha * rhs + alpha_next * direction
    residual = residual - alpha_next * turned
    return (moved + solution, velocity_out, history_new.reshape(hist, rows, cols), residual)


def solution(mesh):
    return jax.shard_map(
        shards,
        mesh=mesh,
        in_specs=(
            P(None, "px", "py"),
            P(None, "px", "py"),
            P(None, "px", "py"),
            P(None, "px", "py"),
            P(None, "px", "py"),
            P(None, "px", "py"),
            P("px", "py", None, None),
            P(),
            P(),
            P("px", "py", None),
        ),
        out_specs=(
            P(None, "px", "py"),
            P(None, "px", "py"),
            P(None, "px", "py"),
            P(None, "px", "py"),
        ),
        check_vma=False,
    )
```

```python
import jax
import jax.numpy as jnp
from jax import lax
from jax.sharding import PartitionSpec as P

ITERS = 2


HIGH = lax.Precision.HIGHEST
STEP = 0.2
CORNERS = ((0, 0), (1, 0), (0, 1), (1, 1))


def with_halo(shard, before, after):
    for axis, dim in (("px", 1), ("py", 2)):
        devices, length = (lax.axis_size(axis), shard.shape[dim])
        up = [(i, i + 1) for i in range(devices - 1)]
        down = [(j, i) for i, j in up]
        parts = [shard]
        if before:
            last = lax.slice_in_dim(shard, length - before, length, axis=dim)
            parts.insert(0, lax.ppermute(last, axis, up))
        if after:
            leading = lax.slice_in_dim(shard, 0, after, axis=dim)
            parts.append(lax.ppermute(leading, axis, down))
        shard = jnp.concatenate(parts, axis=dim)
    return shard


def all_sum(value):
    for axis in ("px", "py"):
        devices = lax.axis_size(axis)
        stride = 1
        while stride < devices:
            radix = min(4, devices // stride)
            total = value
            for k in range(1, radix):
                pairs = []
                for i in range(devices):
                    digit = (i // stride) % radix
                    pairs.append((i, i + (((digit + k) % radix) - digit) * stride))
                total = total + lax.ppermute(value, axis, pairs)
            value = total
            stride *= radix
    return value


def gather_shells(field):
    rows, cols = (field.shape[1] - 1, field.shape[2] - 1)
    return jnp.concatenate(
        [field[:, dx : dx + rows, dy : dy + cols] for dx, dy in CORNERS], axis=0
    )


def scatter_nodes(forces):
    rows, cols = (forces.shape[1] - 1, forces.shape[2] - 1)
    total = jnp.zeros((6, rows, cols), jnp.float32)
    for index, (dx, dy) in enumerate(CORNERS):
        total = (
            total
            + forces[6 * index : 6 * index + 6, 1 - dx : 1 - dx + rows, 1 - dy : 1 - dy + cols]
        )
    return total


def inside(shape, row_from, col_from, rows_total, cols_total, low_only):
    rows, cols = shape
    row = lax.axis_index("px") * rows_total + row_from + jnp.arange(rows)
    col = lax.axis_index("py") * cols_total + col_from + jnp.arange(cols)
    row_ok = row >= 0
    col_ok = col >= 0
    if not low_only:
        row_ok = row_ok & (row < rows_total * lax.axis_size("px"))
        col_ok = col_ok & (col < cols_total * lax.axis_size("py"))
    return (row_ok[:, None] & col_ok[None, :]).astype(jnp.float32)


def shards(
    displacement,
    velocity,
    load,
    inv_mass,
    history,
    contact_home,
    recv_contact,
    stiff_base,
    strain_map,
    slot_table,
):
    hist = history.shape[0]
    rows, cols = (displacement.shape[1], displacement.shape[2])
    cells = rows * cols

    targets = slot_table.reshape(-1)
    devices = lax.axis_size("px") * lax.axis_size("py")
    width = targets.shape[0] // devices
    held = recv_contact.reshape(hist, devices, width)
    arrived = lax.all_to_all(held, ("px", "py"), split_axis=1, concat_axis=1, tiled=True)

    def with_base(shells):
        return jnp.einsum("ab,bxy->axy", stiff_base, shells, precision=HIGH)

    def shell_keep(forces, offset):
        return forces * inside(forces.shape[1:], offset, offset, rows, cols, True)[None]

    def node_keep(field, offset):
        return field * inside(field.shape[1:], offset, offset, rows, cols, False)[None]

    both = with_halo(jnp.concatenate([displacement, load], axis=0), 3, 3)
    start_shells = gather_shells(both[:6])
    force_wide = scatter_nodes(shell_keep(with_base(start_shells), -3))
    force_start = force_wide[:, 2 : rows + 2, 2 : cols + 2]
    velocity_out = velocity + STEP * inv_mass * (load - force_start)
    moved = displacement + STEP * velocity_out
    own = start_shells[:, 3 : rows + 3, 3 : cols + 3].reshape(24, cells)
    history_new = history.reshape(hist, cells) + jnp.dot(strain_map, own, precision=HIGH)
    rhs_wide = node_keep(both[6:, 1 : rows + 5, 1 : cols + 5] - force_wide, -2)

    contact = (
        contact_home.reshape(hist, cells)
        .at[:, targets]
        .set(arrived.reshape(hist, devices * width), mode="drop")
    )
    weights = (jax.nn.softplus(history_new) * contact).reshape(hist, rows, cols)
    weights_wide = with_halo(weights, 2, 1)

    def operate(field, weights_of, offset):
        shells = gather_shells(field)
        strains = jnp.einsum("hb,bxy->hxy", strain_map, shells, precision=HIGH)
        forces = jnp.einsum("hb,hxy->bxy", strain_map, weights_of * strains, precision=HIGH)
        return scatter_nodes(shell_keep(forces + with_base(shells), offset))

    rhs = rhs_wide[:, 2 : rows + 2, 2 : cols + 2]
    image_wide = node_keep(operate(rhs_wide, weights_wide, -2), -1)
    image = image_wide[:, 1 : rows + 1, 1 : cols + 1]
    again = operate(image_wide, weights_wide[:, 1 : rows + 2, 1 : cols + 2], -1)
    first = all_sum(jnp.stack([jnp.sum(rhs * rhs), jnp.sum(rhs * image)]))
    norm_now, curvature = first[0], first[1]
    alpha = norm_now / curvature
    residual = rhs - alpha * image
    bent = image - alpha * again
    second = all_sum(
        jnp.stack(
            [
                jnp.sum(residual * residual),
                jnp.sum(residual * bent),
                jnp.sum(residual * image),
                jnp.sum(rhs * bent),
            ]
        )
    )
    norm_next = second[0]
    beta = norm_next / norm_now
    direction = residual + beta * rhs
    turned = bent + beta * image
    curvature_next = second[1] + beta * (second[2] + second[3]) + beta * beta * curvature
    alpha_next = norm_next / curvature_next
    solution = alpha * rhs + alpha_next * direction
    residual = residual - alpha_next * turned
    return (moved + solution, velocity_out, history_new.reshape(hist, rows, cols), residual)


def solution(mesh):
    return jax.shard_map(
        shards,
        mesh=mesh,
        in_specs=(
            P(None, "px", "py"),
            P(None, "px", "py"),
            P(None, "px", "py"),
            P(None, "px", "py"),
            P(None, "px", "py"),
            P(None, "px", "py"),
            P("px", "py", None, None),
            P(),
            P(),
            P("px", "py", None),
        ),
        out_specs=(
            P(None, "px", "py"),
            P(None, "px", "py"),
            P(None, "px", "py"),
            P(None, "px", "py"),
        ),
        check_vma=False,
    )
```

```python
import jax
import jax.numpy as jnp
from jax import lax
from jax.sharding import PartitionSpec as P

ITERS = 2


HIGH = lax.Precision.HIGHEST
STEP = 0.2
CORNERS = ((0, 0), (1, 0), (0, 1), (1, 1))


def with_halo(shard, before, after):
    for axis, dim in (("px", 1), ("py", 2)):
        devices, length = (lax.axis_size(axis), shard.shape[dim])
        up = [(i, i + 1) for i in range(devices - 1)]
        down = [(j, i) for i, j in up]
        parts = [shard]
        if before:
            last = lax.slice_in_dim(shard, length - before, length, axis=dim)
            parts.insert(0, lax.ppermute(last, axis, up))
        if after:
            leading = lax.slice_in_dim(shard, 0, after, axis=dim)
            parts.append(lax.ppermute(leading, axis, down))
        shard = jnp.concatenate(parts, axis=dim)
    return shard


def all_sum(value):
    for axis in ("px", "py"):
        devices = lax.axis_size(axis)
        stride = 1
        while stride < devices:
            radix = min(4, devices // stride)
            total = value
            for k in range(1, radix):
                pairs = []
                for i in range(devices):
                    digit = (i // stride) % radix
                    pairs.append((i, i + (((digit + k) % radix) - digit) * stride))
                total = total + lax.ppermute(value, axis, pairs)
            value = total
            stride *= radix
    return value


def gather_shells(field):
    rows, cols = (field.shape[1] - 1, field.shape[2] - 1)
    return jnp.concatenate(
        [field[:, dx : dx + rows, dy : dy + cols] for dx, dy in CORNERS], axis=0
    )


def scatter_nodes(forces):
    rows, cols = (forces.shape[1] - 1, forces.shape[2] - 1)
    total = jnp.zeros((6, rows, cols), jnp.float32)
    for index, (dx, dy) in enumerate(CORNERS):
        total = (
            total
            + forces[6 * index : 6 * index + 6, 1 - dx : 1 - dx + rows, 1 - dy : 1 - dy + cols]
        )
    return total


def inside(shape, row_from, col_from, rows_total, cols_total, low_only):
    rows, cols = shape
    row = lax.axis_index("px") * rows_total + row_from + jnp.arange(rows)
    col = lax.axis_index("py") * cols_total + col_from + jnp.arange(cols)
    row_ok = row >= 0
    col_ok = col >= 0
    if not low_only:
        row_ok = row_ok & (row < rows_total * lax.axis_size("px"))
        col_ok = col_ok & (col < cols_total * lax.axis_size("py"))
    return (row_ok[:, None] & col_ok[None, :]).astype(jnp.float32)


def shards(
    displacement,
    velocity,
    load,
    inv_mass,
    history,
    contact_home,
    recv_contact,
    stiff_base,
    strain_map,
    slot_table,
):
    hist = history.shape[0]
    rows, cols = (displacement.shape[1], displacement.shape[2])
    cells = rows * cols

    targets = slot_table.reshape(-1)
    devices = lax.axis_size("px") * lax.axis_size("py")
    width = targets.shape[0] // devices
    held = recv_contact.reshape(hist, devices, width)
    arrived = lax.all_to_all(held, ("px", "py"), split_axis=1, concat_axis=1, tiled=True)

    def with_base(shells):
        return jnp.einsum("ab,bxy->axy", stiff_base, shells, precision=HIGH)

    def shell_keep(forces, offset):
        return forces * inside(forces.shape[1:], offset, offset, rows, cols, True)[None]

    def node_keep(field, offset):
        return field * inside(field.shape[1:], offset, offset, rows, cols, False)[None]

    both = with_halo(jnp.concatenate([displacement, load], axis=0), 3, 3)
    start_shells = gather_shells(both[:6])
    force_wide = scatter_nodes(shell_keep(with_base(start_shells), -3))
    force_start = force_wide[:, 2 : rows + 2, 2 : cols + 2]
    velocity_out = velocity + STEP * inv_mass * (load - force_start)
    moved = displacement + STEP * velocity_out
    own = start_shells[:, 3 : rows + 3, 3 : cols + 3].reshape(24, cells)
    history_new = history.reshape(hist, cells) + jnp.dot(strain_map, own, precision=HIGH)
    rhs_wide = node_keep(both[6:, 1 : rows + 5, 1 : cols + 5] - force_wide, -2)

    contact = (
        contact_home.reshape(hist, cells)
        .at[:, targets]
        .set(arrived.reshape(hist, devices * width), mode="drop")
    )
    weights = (jax.nn.softplus(history_new) * contact).reshape(hist, rows, cols)
    weights_wide = with_halo(weights, 2, 1)

    def operate(field, weights_of, offset):
        shells = gather_shells(field)
        strains = jnp.einsum("hb,bxy->hxy", strain_map, shells, precision=HIGH)
        forces = jnp.einsum("hb,hxy->bxy", strain_map, weights_of * strains, precision=HIGH)
        return scatter_nodes(shell_keep(forces + with_base(shells), offset))

    rhs = rhs_wide[:, 2 : rows + 2, 2 : cols + 2]
    own_rhs = gather_shells(rhs_wide[:, 2 : rows + 3, 2 : cols + 3])
    own_rhs_base = with_base(own_rhs)
    own_rhs_strain = jnp.einsum("hb,bxy->hxy", strain_map, own_rhs, precision=HIGH)
    first = all_sum(
        jnp.stack(
            [
                jnp.sum(rhs * rhs),
                jnp.sum(own_rhs * own_rhs_base) + jnp.sum(weights * own_rhs_strain * own_rhs_strain),
            ]
        )
    )
    image_wide = node_keep(operate(rhs_wide, weights_wide, -2), -1)
    image = image_wide[:, 1 : rows + 1, 1 : cols + 1]
    again = operate(image_wide, weights_wide[:, 1 : rows + 2, 1 : cols + 2], -1)
    own_image = gather_shells(image_wide[:, 1 : rows + 2, 1 : cols + 2])
    own_image_base = with_base(own_image)
    own_image_strain = jnp.einsum("hb,bxy->hxy", strain_map, own_image, precision=HIGH)
    norm_now, curvature = first[0], first[1]
    alpha = norm_now / curvature
    residual = rhs - alpha * image
    own_res = own_rhs - alpha * own_image
    own_res_base = own_rhs_base - alpha * own_image_base
    own_res_strain = own_rhs_strain - alpha * own_image_strain
    second = all_sum(
        jnp.stack(
            [
                jnp.sum(residual * residual),
                jnp.sum(own_res * own_res_base)
                + jnp.sum(weights * own_res_strain * own_res_strain),
                jnp.sum(own_res * own_rhs_base)
                + jnp.sum(weights * own_res_strain * own_rhs_strain),
            ]
        )
    )
    norm_next = second[0]
    beta = norm_next / norm_now
    direction = residual + beta * rhs
    turned = image - alpha * again + beta * image
    curvature_next = second[1] + 2.0 * beta * second[2] + beta * beta * curvature
    alpha_next = norm_next / curvature_next
    solution = alpha * rhs + alpha_next * direction
    residual = residual - alpha_next * turned
    return (moved + solution, velocity_out, history_new.reshape(hist, rows, cols), residual)


def solution(mesh):
    return jax.shard_map(
        shards,
        mesh=mesh,
        in_specs=(
            P(None, "px", "py"),
            P(None, "px", "py"),
            P(None, "px", "py"),
            P(None, "px", "py"),
            P(None, "px", "py"),
            P(None, "px", "py"),
            P("px", "py", None, None),
            P(),
            P(),
            P("px", "py", None),
        ),
        out_specs=(
            P(None, "px", "py"),
            P(None, "px", "py"),
            P(None, "px", "py"),
            P(None, "px", "py"),
        ),
        check_vma=False,
    )
```

```python
import jax
import jax.numpy as jnp
from jax import lax
from jax.sharding import PartitionSpec as P

ITERS = 2


HIGH = lax.Precision.HIGHEST
STEP = 0.2
CORNERS = ((0, 0), (1, 0), (0, 1), (1, 1))


def with_halo(shard, before, after):
    for axis, dim in (("px", 1), ("py", 2)):
        devices, length = (lax.axis_size(axis), shard.shape[dim])
        up = [(i, i + 1) for i in range(devices - 1)]
        down = [(j, i) for i, j in up]
        parts = [shard]
        if before:
            last = lax.slice_in_dim(shard, length - before, length, axis=dim)
            parts.insert(0, lax.ppermute(last, axis, up))
        if after:
            leading = lax.slice_in_dim(shard, 0, after, axis=dim)
            parts.append(lax.ppermute(leading, axis, down))
        shard = jnp.concatenate(parts, axis=dim)
    return shard


def all_sum(value):
    for axis in ("px", "py"):
        devices = lax.axis_size(axis)
        stride = 1
        while stride < devices:
            radix = min(4, devices // stride)
            total = value
            for k in range(1, radix):
                pairs = []
                for i in range(devices):
                    digit = (i // stride) % radix
                    pairs.append((i, i + (((digit + k) % radix) - digit) * stride))
                total = total + lax.ppermute(value, axis, pairs)
            value = total
            stride *= radix
    return value


def gather_shells(field):
    rows, cols = (field.shape[1] - 1, field.shape[2] - 1)
    return jnp.concatenate(
        [field[:, dx : dx + rows, dy : dy + cols] for dx, dy in CORNERS], axis=0
    )


def scatter_nodes(forces):
    rows, cols = (forces.shape[1] - 1, forces.shape[2] - 1)
    total = jnp.zeros((6, rows, cols), jnp.float32)
    for index, (dx, dy) in enumerate(CORNERS):
        total = (
            total
            + forces[6 * index : 6 * index + 6, 1 - dx : 1 - dx + rows, 1 - dy : 1 - dy + cols]
        )
    return total


def inside(shape, row_from, col_from, rows_total, cols_total, low_only):
    rows, cols = shape
    row = lax.axis_index("px") * rows_total + row_from + jnp.arange(rows)
    col = lax.axis_index("py") * cols_total + col_from + jnp.arange(cols)
    row_ok = row >= 0
    col_ok = col >= 0
    if not low_only:
        row_ok = row_ok & (row < rows_total * lax.axis_size("px"))
        col_ok = col_ok & (col < cols_total * lax.axis_size("py"))
    return (row_ok[:, None] & col_ok[None, :]).astype(jnp.float32)


def shards(
    displacement,
    velocity,
    load,
    inv_mass,
    history,
    contact_home,
    recv_contact,
    stiff_base,
    strain_map,
    slot_table,
):
    hist = history.shape[0]
    rows, cols = (displacement.shape[1], displacement.shape[2])
    cells = rows * cols

    targets = slot_table.reshape(-1)
    devices = lax.axis_size("px") * lax.axis_size("py")
    width = targets.shape[0] // devices
    held = recv_contact.reshape(hist, devices, width)
    arrived = lax.all_to_all(held, ("px", "py"), split_axis=1, concat_axis=1, tiled=True)

    def with_base(shells):
        return jnp.einsum("ab,bxy->axy", stiff_base, shells, precision=HIGH)

    def shell_keep(forces, offset):
        return forces * inside(forces.shape[1:], offset, offset, rows, cols, True)[None]

    def node_keep(field, offset):
        return field * inside(field.shape[1:], offset, offset, rows, cols, False)[None]

    both = with_halo(jnp.concatenate([displacement, load], axis=0), 3, 3)
    start_shells = gather_shells(both[:6])
    force_wide = scatter_nodes(shell_keep(with_base(start_shells), -3))
    force_start = force_wide[:, 2 : rows + 2, 2 : cols + 2]
    velocity_out = velocity + STEP * inv_mass * (load - force_start)
    moved = displacement + STEP * velocity_out
    own = start_shells[:, 3 : rows + 3, 3 : cols + 3].reshape(24, cells)
    history_new = history.reshape(hist, cells) + jnp.dot(strain_map, own, precision=HIGH)
    rhs_wide = node_keep(both[6:, 1 : rows + 5, 1 : cols + 5] - force_wide, -2)

    soft = jax.nn.softplus(history_new)
    soft_relaid = jnp.take(soft, targets, axis=1, mode="fill", fill_value=0.0)
    weights_home, soft_relaid = lax.optimization_barrier(
        (soft * contact_home.reshape(hist, cells), soft_relaid)
    )
    weights = (
        weights_home.at[:, targets]
        .set(soft_relaid * arrived.reshape(hist, devices * width), mode="drop")
        .reshape(hist, rows, cols)
    )
    weights_wide = with_halo(weights, 2, 1)

    def operate(field, weights_of, offset):
        shells = gather_shells(field)
        strains = jnp.einsum("hb,bxy->hxy", strain_map, shells, precision=HIGH)
        forces = jnp.einsum("hb,hxy->bxy", strain_map, weights_of * strains, precision=HIGH)
        return scatter_nodes(shell_keep(forces + with_base(shells), offset))

    rhs = rhs_wide[:, 2 : rows + 2, 2 : cols + 2]
    image_wide = node_keep(operate(rhs_wide, weights_wide, -2), -1)
    image = image_wide[:, 1 : rows + 1, 1 : cols + 1]
    again = operate(image_wide, weights_wide[:, 1 : rows + 2, 1 : cols + 2], -1)
    first = all_sum(jnp.stack([jnp.sum(rhs * rhs), jnp.sum(rhs * image)]))
    norm_now, curvature = first[0], first[1]
    alpha = norm_now / curvature
    residual = rhs - alpha * image
    bent = image - alpha * again
    second = all_sum(
        jnp.stack(
            [
                jnp.sum(residual * residual),
                jnp.sum(residual * bent),
                jnp.sum(residual * image),
                jnp.sum(rhs * bent),
            ]
        )
    )
    norm_next = second[0]
    beta = norm_next / norm_now
    direction = residual + beta * rhs
    turned = bent + beta * image
    curvature_next = second[1] + beta * (second[2] + second[3]) + beta * beta * curvature
    alpha_next = norm_next / curvature_next
    solution = alpha * rhs + alpha_next * direction
    residual = residual - alpha_next * turned
    return (moved + solution, velocity_out, history_new.reshape(hist, rows, cols), residual)


def solution(mesh):
    return jax.shard_map(
        shards,
        mesh=mesh,
        in_specs=(
            P(None, "px", "py"),
            P(None, "px", "py"),
            P(None, "px", "py"),
            P(None, "px", "py"),
            P(None, "px", "py"),
            P(None, "px", "py"),
            P("px", "py", None, None),
            P(),
            P(),
            P("px", "py", None),
        ),
        out_specs=(
            P(None, "px", "py"),
            P(None, "px", "py"),
            P(None, "px", "py"),
            P(None, "px", "py"),
        ),
        check_vma=False,
    )
```

```python
import jax
import jax.numpy as jnp
from jax import lax
from jax.sharding import PartitionSpec as P

ITERS = 2


HIGH = lax.Precision.HIGHEST
STEP = 0.2
CORNERS = ((0, 0), (1, 0), (0, 1), (1, 1))


def with_halo(shard, before, after):
    for axis, dim in (("px", 1), ("py", 2)):
        devices, length = (lax.axis_size(axis), shard.shape[dim])
        up = [(i, i + 1) for i in range(devices - 1)]
        down = [(j, i) for i, j in up]
        parts = [shard]
        if before:
            last = lax.slice_in_dim(shard, length - before, length, axis=dim)
            parts.insert(0, lax.ppermute(last, axis, up))
        if after:
            leading = lax.slice_in_dim(shard, 0, after, axis=dim)
            parts.append(lax.ppermute(leading, axis, down))
        shard = jnp.concatenate(parts, axis=dim)
    return shard


def all_sum(value):
    for axis in ("px", "py"):
        devices = lax.axis_size(axis)
        stride = 1
        while stride < devices:
            radix = min(4, devices // stride)
            total = value
            for k in range(1, radix):
                pairs = []
                for i in range(devices):
                    digit = (i // stride) % radix
                    pairs.append((i, i + (((digit + k) % radix) - digit) * stride))
                total = total + lax.ppermute(value, axis, pairs)
            value = total
            stride *= radix
    return value


def gather_shells(field):
    rows, cols = (field.shape[1] - 1, field.shape[2] - 1)
    return jnp.concatenate(
        [field[:, dx : dx + rows, dy : dy + cols] for dx, dy in CORNERS], axis=0
    )


def scatter_nodes(forces):
    rows, cols = (forces.shape[1] - 1, forces.shape[2] - 1)
    total = jnp.zeros((6, rows, cols), jnp.float32)
    for index, (dx, dy) in enumerate(CORNERS):
        total = (
            total
            + forces[6 * index : 6 * index + 6, 1 - dx : 1 - dx + rows, 1 - dy : 1 - dy + cols]
        )
    return total


def inside(shape, row_from, col_from, rows_total, cols_total, low_only):
    rows, cols = shape
    row = lax.axis_index("px") * rows_total + row_from + jnp.arange(rows)
    col = lax.axis_index("py") * cols_total + col_from + jnp.arange(cols)
    row_ok = row >= 0
    col_ok = col >= 0
    if not low_only:
        row_ok = row_ok & (row < rows_total * lax.axis_size("px"))
        col_ok = col_ok & (col < cols_total * lax.axis_size("py"))
    return (row_ok[:, None] & col_ok[None, :]).astype(jnp.float32)


def shards(
    displacement,
    velocity,
    load,
    inv_mass,
    history,
    contact_home,
    recv_contact,
    stiff_base,
    strain_map,
    slot_table,
):
    hist = history.shape[0]
    rows, cols = (displacement.shape[1], displacement.shape[2])
    cells = rows * cols

    targets = slot_table.reshape(-1)
    devices = lax.axis_size("px") * lax.axis_size("py")
    width = targets.shape[0] // devices
    held = recv_contact.reshape(hist, lax.axis_size("px"), lax.axis_size("py"), width)
    held = lax.all_to_all(held, "py", split_axis=2, concat_axis=2, tiled=True)
    arrived = lax.all_to_all(held, "px", split_axis=1, concat_axis=1, tiled=True)

    def with_base(shells):
        return jnp.einsum("ab,bxy->axy", stiff_base, shells, precision=HIGH)

    def shell_keep(forces, offset):
        return forces * inside(forces.shape[1:], offset, offset, rows, cols, True)[None]

    def node_keep(field, offset):
        return field * inside(field.shape[1:], offset, offset, rows, cols, False)[None]

    both = with_halo(jnp.concatenate([displacement, load], axis=0), 3, 3)
    start_shells = gather_shells(both[:6])
    force_wide = scatter_nodes(shell_keep(with_base(start_shells), -3))
    force_start = force_wide[:, 2 : rows + 2, 2 : cols + 2]
    velocity_out = velocity + STEP * inv_mass * (load - force_start)
    moved = displacement + STEP * velocity_out
    own = start_shells[:, 3 : rows + 3, 3 : cols + 3].reshape(24, cells)
    history_new = history.reshape(hist, cells) + jnp.dot(strain_map, own, precision=HIGH)
    rhs_wide = node_keep(both[6:, 1 : rows + 5, 1 : cols + 5] - force_wide, -2)

    contact = (
        contact_home.reshape(hist, cells)
        .at[:, targets]
        .set(arrived.reshape(hist, devices * width), mode="drop")
    )
    weights = (jax.nn.softplus(history_new) * contact).reshape(hist, rows, cols)
    weights_wide = with_halo(weights, 2, 1)

    def operate(field, weights_of, offset):
        shells = gather_shells(field)
        strains = jnp.einsum("hb,bxy->hxy", strain_map, shells, precision=HIGH)
        forces = jnp.einsum("hb,hxy->bxy", strain_map, weights_of * strains, precision=HIGH)
        return scatter_nodes(shell_keep(forces + with_base(shells), offset))

    rhs = rhs_wide[:, 2 : rows + 2, 2 : cols + 2]
    image_wide = node_keep(operate(rhs_wide, weights_wide, -2), -1)
    image = image_wide[:, 1 : rows + 1, 1 : cols + 1]
    again = operate(image_wide, weights_wide[:, 1 : rows + 2, 1 : cols + 2], -1)
    first = all_sum(jnp.stack([jnp.sum(rhs * rhs), jnp.sum(rhs * image)]))
    norm_now, curvature = first[0], first[1]
    alpha = norm_now / curvature
    residual = rhs - alpha * image
    bent = image - alpha * again
    second = all_sum(
        jnp.stack(
            [
                jnp.sum(residual * residual),
                jnp.sum(residual * bent),
                jnp.sum(residual * image),
                jnp.sum(rhs * bent),
            ]
        )
    )
    norm_next = second[0]
    beta = norm_next / norm_now
    direction = residual + beta * rhs
    turned = bent + beta * image
    curvature_next = second[1] + beta * (second[2] + second[3]) + beta * beta * curvature
    alpha_next = norm_next / curvature_next
    solution = alpha * rhs + alpha_next * direction
    residual = residual - alpha_next * turned
    return (moved + solution, velocity_out, history_new.reshape(hist, rows, cols), residual)


def solution(mesh):
    return jax.shard_map(
        shards,
        mesh=mesh,
        in_specs=(
            P(None, "px", "py"),
            P(None, "px", "py"),
            P(None, "px", "py"),
            P(None, "px", "py"),
            P(None, "px", "py"),
            P(None, "px", "py"),
            P("px", "py", None, None),
            P(),
            P(),
            P("px", "py", None),
        ),
        out_specs=(
            P(None, "px", "py"),
            P(None, "px", "py"),
            P(None, "px", "py"),
            P(None, "px", "py"),
        ),
        check_vma=False,
    )
```

```python
import jax
import jax.numpy as jnp
from jax import lax
from jax.sharding import PartitionSpec as P

ITERS = 2


HIGH = lax.Precision.HIGHEST
STEP = 0.2
CORNERS = ((0, 0), (1, 0), (0, 1), (1, 1))


def with_halo(shard, before, after):
    for axis, dim in (("px", 1), ("py", 2)):
        devices, length = (lax.axis_size(axis), shard.shape[dim])
        up = [(i, i + 1) for i in range(devices - 1)]
        down = [(j, i) for i, j in up]
        parts = [shard]
        if before:
            last = lax.slice_in_dim(shard, length - before, length, axis=dim)
            parts.insert(0, lax.ppermute(last, axis, up))
        if after:
            leading = lax.slice_in_dim(shard, 0, after, axis=dim)
            parts.append(lax.ppermute(leading, axis, down))
        shard = jnp.concatenate(parts, axis=dim)
    return shard


def all_sum(value):
    for axis in ("px", "py"):
        devices = lax.axis_size(axis)
        stride = 1
        while stride < devices:
            radix = min(4, devices // stride)
            total = value
            for k in range(1, radix):
                pairs = []
                for i in range(devices):
                    digit = (i // stride) % radix
                    pairs.append((i, i + (((digit + k) % radix) - digit) * stride))
                total = total + lax.ppermute(value, axis, pairs)
            value = total
            stride *= radix
    return value


def gather_shells(field):
    rows, cols = (field.shape[1] - 1, field.shape[2] - 1)
    return jnp.concatenate(
        [field[:, dx : dx + rows, dy : dy + cols] for dx, dy in CORNERS], axis=0
    )


def scatter_nodes(forces):
    rows, cols = (forces.shape[1] - 1, forces.shape[2] - 1)
    total = jnp.zeros((6, rows, cols), jnp.float32)
    for index, (dx, dy) in enumerate(CORNERS):
        total = (
            total
            + forces[6 * index : 6 * index + 6, 1 - dx : 1 - dx + rows, 1 - dy : 1 - dy + cols]
        )
    return total


def inside(shape, row_from, col_from, rows_total, cols_total, low_only):
    rows, cols = shape
    row = lax.axis_index("px") * rows_total + row_from + jnp.arange(rows)
    col = lax.axis_index("py") * cols_total + col_from + jnp.arange(cols)
    row_ok = row >= 0
    col_ok = col >= 0
    if not low_only:
        row_ok = row_ok & (row < rows_total * lax.axis_size("px"))
        col_ok = col_ok & (col < cols_total * lax.axis_size("py"))
    return (row_ok[:, None] & col_ok[None, :]).astype(jnp.float32)


def shards(
    displacement,
    velocity,
    load,
    inv_mass,
    history,
    contact_home,
    recv_contact,
    stiff_base,
    strain_map,
    slot_table,
):
    hist = history.shape[0]
    rows, cols = (displacement.shape[1], displacement.shape[2])
    cells = rows * cols

    targets = slot_table.reshape(-1)
    devices = lax.axis_size("px") * lax.axis_size("py")
    width = targets.shape[0] // devices
    held = recv_contact.reshape(hist, devices, width)
    arrived = lax.all_to_all(held, ("px", "py"), split_axis=1, concat_axis=1, tiled=True)

    def with_base(shells):
        return jnp.einsum("ab,bxy->axy", stiff_base, shells, precision=HIGH)

    def shell_keep(forces, offset):
        return forces * inside(forces.shape[1:], offset, offset, rows, cols, True)[None]

    def node_keep(field, offset):
        return field * inside(field.shape[1:], offset, offset, rows, cols, False)[None]

    both = with_halo(jnp.concatenate([displacement, load], axis=0), 3, 3)
    start_shells = gather_shells(both[:6])
    force_wide = scatter_nodes(shell_keep(with_base(start_shells), -3))
    force_start = force_wide[:, 2 : rows + 2, 2 : cols + 2]
    velocity_out = velocity + STEP * inv_mass * (load - force_start)
    moved = displacement + STEP * velocity_out
    own = start_shells[:, 3 : rows + 3, 3 : cols + 3].reshape(24, cells)
    history_new = history.reshape(hist, cells) + jnp.dot(strain_map, own, precision=HIGH)
    rhs_wide = node_keep(both[6:, 1 : rows + 5, 1 : cols + 5] - force_wide, -2)

    contact = (
        contact_home.reshape(hist, cells)
        .at[:, targets]
        .set(arrived.reshape(hist, devices * width), mode="drop")
    )
    weights = (jax.nn.softplus(history_new) * contact).reshape(hist, rows, cols)
    weights_wide = with_halo(weights, 2, 1)

    def operate(field, weights_of, offset):
        shells = gather_shells(field)
        strains = jnp.einsum("hb,bxy->hxy", strain_map, shells, precision=HIGH)
        forces = jnp.einsum("hb,hxy->bxy", strain_map, weights_of * strains, precision=HIGH)
        return scatter_nodes(shell_keep(forces + with_base(shells), offset))

    rhs = rhs_wide[:, 2 : rows + 2, 2 : cols + 2]
    image_wide = node_keep(operate(rhs_wide, weights_wide, -2), -1)
    image = image_wide[:, 1 : rows + 1, 1 : cols + 1]
    again = operate(image_wide, weights_wide[:, 1 : rows + 2, 1 : cols + 2], -1)
    def lanes(values):
        values = jnp.stack(values)
        return jnp.broadcast_to(values[:, None], (values.shape[0], cols))

    first = all_sum(lanes([jnp.sum(rhs * rhs), jnp.sum(rhs * image)]))
    norm_now, curvature = first[0], first[1]
    alpha = norm_now / curvature
    residual = rhs - alpha * image
    bent = image - alpha * again
    second = all_sum(
        lanes(
            [
                jnp.sum(residual * residual),
                jnp.sum(residual * bent),
                jnp.sum(residual * image),
                jnp.sum(rhs * bent),
            ]
        )
    )
    norm_next = second[0]
    beta = norm_next / norm_now
    direction = residual + beta * rhs
    turned = bent + beta * image
    curvature_next = second[1] + beta * (second[2] + second[3]) + beta * beta * curvature
    alpha_next = norm_next / curvature_next
    solution = alpha * rhs + alpha_next * direction
    residual = residual - alpha_next * turned
    return (moved + solution, velocity_out, history_new.reshape(hist, rows, cols), residual)


def solution(mesh):
    return jax.shard_map(
        shards,
        mesh=mesh,
        in_specs=(
            P(None, "px", "py"),
            P(None, "px", "py"),
            P(None, "px", "py"),
            P(None, "px", "py"),
            P(None, "px", "py"),
            P(None, "px", "py"),
            P("px", "py", None, None),
            P(),
            P(),
            P("px", "py", None),
        ),
        out_specs=(
            P(None, "px", "py"),
            P(None, "px", "py"),
            P(None, "px", "py"),
            P(None, "px", "py"),
        ),
        check_vma=False,
    )
```

```python
import jax
import jax.numpy as jnp
from jax import lax
from jax.sharding import PartitionSpec as P

ITERS = 2


HIGH = lax.Precision.HIGHEST
STEP = 0.2
CORNERS = ((0, 0), (1, 0), (0, 1), (1, 1))


def with_halo(shard, before, after):
    for axis, dim in (("px", 1), ("py", 2)):
        devices, length = (lax.axis_size(axis), shard.shape[dim])
        up = [(i, i + 1) for i in range(devices - 1)]
        down = [(j, i) for i, j in up]
        parts = [shard]
        if before:
            last = lax.slice_in_dim(shard, length - before, length, axis=dim)
            parts.insert(0, lax.ppermute(last, axis, up))
        if after:
            leading = lax.slice_in_dim(shard, 0, after, axis=dim)
            parts.append(lax.ppermute(leading, axis, down))
        shard = jnp.concatenate(parts, axis=dim)
    return shard


def all_sum(value):
    for axis in ("px", "py"):
        devices = lax.axis_size(axis)
        stride = 1
        while stride < devices:
            radix = min(4, devices // stride)
            total = value
            for k in range(1, radix):
                pairs = []
                for i in range(devices):
                    digit = (i // stride) % radix
                    pairs.append((i, i + (((digit + k) % radix) - digit) * stride))
                total = total + lax.ppermute(value, axis, pairs)
            value = total
            stride *= radix
    return value


def gather_shells(field):
    rows, cols = (field.shape[1] - 1, field.shape[2] - 1)
    return jnp.concatenate(
        [field[:, dx : dx + rows, dy : dy + cols] for dx, dy in CORNERS], axis=0
    )


def scatter_nodes(forces):
    rows, cols = (forces.shape[1] - 1, forces.shape[2] - 1)
    total = jnp.zeros((6, rows, cols), jnp.float32)
    for index, (dx, dy) in enumerate(CORNERS):
        total = (
            total
            + forces[6 * index : 6 * index + 6, 1 - dx : 1 - dx + rows, 1 - dy : 1 - dy + cols]
        )
    return total


def inside(shape, row_from, col_from, rows_total, cols_total, low_only):
    rows, cols = shape
    row = lax.axis_index("px") * rows_total + row_from + jnp.arange(rows)
    col = lax.axis_index("py") * cols_total + col_from + jnp.arange(cols)
    row_ok = row >= 0
    col_ok = col >= 0
    if not low_only:
        row_ok = row_ok & (row < rows_total * lax.axis_size("px"))
        col_ok = col_ok & (col < cols_total * lax.axis_size("py"))
    return (row_ok[:, None] & col_ok[None, :]).astype(jnp.float32)


def shards(
    displacement,
    velocity,
    load,
    inv_mass,
    history,
    contact_home,
    recv_contact,
    stiff_base,
    strain_map,
    slot_table,
):
    hist = history.shape[0]
    rows, cols = (displacement.shape[1], displacement.shape[2])
    cells = rows * cols

    targets = slot_table.reshape(-1)
    devices = lax.axis_size("px") * lax.axis_size("py")
    width = targets.shape[0] // devices
    held = recv_contact.reshape(hist, devices, width)
    arrived = lax.all_to_all(held, ("px", "py"), split_axis=1, concat_axis=1, tiled=True)

    def with_base(shells):
        return jnp.einsum("ab,bxy->axy", stiff_base, shells, precision=HIGH)

    shell_mask = inside((rows + 5, cols + 5), -3, -3, rows, cols, True)
    node_mask = inside((rows + 4, cols + 4), -2, -2, rows, cols, False)

    def shell_keep(forces, offset):
        skip = offset + 3
        return forces * shell_mask[None, skip : skip + forces.shape[1], skip : skip + forces.shape[2]]

    def node_keep(field, offset):
        skip = offset + 2
        return field * node_mask[None, skip : skip + field.shape[1], skip : skip + field.shape[2]]

    both = with_halo(jnp.concatenate([displacement, load], axis=0), 3, 3)
    start_shells = gather_shells(both[:6])
    force_wide = scatter_nodes(shell_keep(with_base(start_shells), -3))
    force_start = force_wide[:, 2 : rows + 2, 2 : cols + 2]
    velocity_out = velocity + STEP * inv_mass * (load - force_start)
    moved = displacement + STEP * velocity_out
    own = start_shells[:, 3 : rows + 3, 3 : cols + 3].reshape(24, cells)
    history_new = history.reshape(hist, cells) + jnp.dot(strain_map, own, precision=HIGH)
    rhs_wide = node_keep(both[6:, 1 : rows + 5, 1 : cols + 5] - force_wide, -2)

    contact = (
        contact_home.reshape(hist, cells)
        .at[:, targets]
        .set(arrived.reshape(hist, devices * width), mode="drop")
    )
    weights = (jax.nn.softplus(history_new) * contact).reshape(hist, rows, cols)
    weights_wide = with_halo(weights, 2, 1)

    def operate(field, weights_of, offset):
        shells = gather_shells(field)
        strains = jnp.einsum("hb,bxy->hxy", strain_map, shells, precision=HIGH)
        forces = jnp.einsum("hb,hxy->bxy", strain_map, weights_of * strains, precision=HIGH)
        return scatter_nodes(shell_keep(forces + with_base(shells), offset))

    rhs = rhs_wide[:, 2 : rows + 2, 2 : cols + 2]
    image_wide = node_keep(operate(rhs_wide, weights_wide, -2), -1)
    image = image_wide[:, 1 : rows + 1, 1 : cols + 1]
    again = operate(image_wide, weights_wide[:, 1 : rows + 2, 1 : cols + 2], -1)
    def lanes(values):
        values = jnp.stack(values)
        return jnp.broadcast_to(values[:, None], (values.shape[0], cols))

    first = all_sum(lanes([jnp.sum(rhs * rhs), jnp.sum(rhs * image)]))
    norm_now, curvature = first[0], first[1]
    alpha = norm_now / curvature
    residual = rhs - alpha * image
    bent = image - alpha * again
    second = all_sum(
        lanes(
            [
                jnp.sum(residual * residual),
                jnp.sum(residual * bent),
                jnp.sum(residual * image),
                jnp.sum(rhs * bent),
            ]
        )
    )
    norm_next = second[0]
    beta = norm_next / norm_now
    direction = residual + beta * rhs
    turned = bent + beta * image
    curvature_next = second[1] + beta * (second[2] + second[3]) + beta * beta * curvature
    alpha_next = norm_next / curvature_next
    solution = alpha * rhs + alpha_next * direction
    residual = residual - alpha_next * turned
    return (moved + solution, velocity_out, history_new.reshape(hist, rows, cols), residual)


def solution(mesh):
    return jax.shard_map(
        shards,
        mesh=mesh,
        in_specs=(
            P(None, "px", "py"),
            P(None, "px", "py"),
            P(None, "px", "py"),
            P(None, "px", "py"),
            P(None, "px", "py"),
            P(None, "px", "py"),
            P("px", "py", None, None),
            P(),
            P(),
            P("px", "py", None),
        ),
        out_specs=(
            P(None, "px", "py"),
            P(None, "px", "py"),
            P(None, "px", "py"),
            P(None, "px", "py"),
        ),
        check_vma=False,
    )
```

```python
import jax
import jax.numpy as jnp
from jax import lax
from jax.sharding import PartitionSpec as P

ITERS = 2


HIGH = lax.Precision.HIGHEST
STEP = 0.2
CORNERS = ((0, 0), (1, 0), (0, 1), (1, 1))


def with_halo(shard, before, after, sides=(("px", 1), ("py", 2))):
    for axis, dim in sides:
        devices, length = (lax.axis_size(axis), shard.shape[dim])
        up = [(i, i + 1) for i in range(devices - 1)]
        down = [(j, i) for i, j in up]
        parts = [shard]
        if before:
            last = lax.slice_in_dim(shard, length - before, length, axis=dim)
            parts.insert(0, lax.ppermute(last, axis, up))
        if after:
            leading = lax.slice_in_dim(shard, 0, after, axis=dim)
            parts.append(lax.ppermute(leading, axis, down))
        shard = jnp.concatenate(parts, axis=dim)
    return shard


def all_sum(value):
    for axis in ("px", "py"):
        devices = lax.axis_size(axis)
        stride = 1
        while stride < devices:
            radix = min(4, devices // stride)
            total = value
            for k in range(1, radix):
                pairs = []
                for i in range(devices):
                    digit = (i // stride) % radix
                    pairs.append((i, i + (((digit + k) % radix) - digit) * stride))
                total = total + lax.ppermute(value, axis, pairs)
            value = total
            stride *= radix
    return value


def gather_shells(field):
    rows, cols = (field.shape[1] - 1, field.shape[2] - 1)
    return jnp.concatenate(
        [field[:, dx : dx + rows, dy : dy + cols] for dx, dy in CORNERS], axis=0
    )


def scatter_nodes(forces):
    rows, cols = (forces.shape[1] - 1, forces.shape[2] - 1)
    total = jnp.zeros((6, rows, cols), jnp.float32)
    for index, (dx, dy) in enumerate(CORNERS):
        total = (
            total
            + forces[6 * index : 6 * index + 6, 1 - dx : 1 - dx + rows, 1 - dy : 1 - dy + cols]
        )
    return total


def inside(shape, row_from, col_from, rows_total, cols_total, low_only):
    rows, cols = shape
    row = lax.axis_index("px") * rows_total + row_from + jnp.arange(rows)
    col = lax.axis_index("py") * cols_total + col_from + jnp.arange(cols)
    row_ok = row >= 0
    col_ok = col >= 0
    if not low_only:
        row_ok = row_ok & (row < rows_total * lax.axis_size("px"))
        col_ok = col_ok & (col < cols_total * lax.axis_size("py"))
    return (row_ok[:, None] & col_ok[None, :]).astype(jnp.float32)


def shards(
    displacement,
    velocity,
    load,
    inv_mass,
    history,
    contact_home,
    recv_contact,
    stiff_base,
    strain_map,
    slot_table,
):
    hist = history.shape[0]
    rows, cols = (displacement.shape[1], displacement.shape[2])
    cells = rows * cols

    targets = slot_table.reshape(-1)
    devices = lax.axis_size("px") * lax.axis_size("py")
    width = targets.shape[0] // devices
    held = recv_contact.reshape(hist, devices, width)
    arrived = lax.all_to_all(held, ("px", "py"), split_axis=1, concat_axis=1, tiled=True)

    def with_base(shells):
        return jnp.einsum("ab,bxy->axy", stiff_base, shells, precision=HIGH)

    def shell_keep(forces, offset):
        return forces * inside(forces.shape[1:], offset, offset, rows, cols, True)[None]

    def node_keep(field, offset):
        return field * inside(field.shape[1:], offset, offset, rows, cols, False)[None]

    both = with_halo(jnp.concatenate([displacement, load], axis=0), 3, 3, (("px", 1),))
    both, arrived = lax.optimization_barrier((both, arrived))
    both = with_halo(both, 3, 3, (("py", 2),))
    start_shells = gather_shells(both[:6])
    force_wide = scatter_nodes(shell_keep(with_base(start_shells), -3))
    force_start = force_wide[:, 2 : rows + 2, 2 : cols + 2]
    velocity_out = velocity + STEP * inv_mass * (load - force_start)
    moved = displacement + STEP * velocity_out
    own = start_shells[:, 3 : rows + 3, 3 : cols + 3].reshape(24, cells)
    history_new = history.reshape(hist, cells) + jnp.dot(strain_map, own, precision=HIGH)
    rhs_wide = node_keep(both[6:, 1 : rows + 5, 1 : cols + 5] - force_wide, -2)

    contact = (
        contact_home.reshape(hist, cells)
        .at[:, targets]
        .set(arrived.reshape(hist, devices * width), mode="drop")
    )
    weights = (jax.nn.softplus(history_new) * contact).reshape(hist, rows, cols)
    weights_wide = with_halo(weights, 2, 1)

    def operate(field, weights_of, offset):
        shells = gather_shells(field)
        strains = jnp.einsum("hb,bxy->hxy", strain_map, shells, precision=HIGH)
        forces = jnp.einsum("hb,hxy->bxy", strain_map, weights_of * strains, precision=HIGH)
        return scatter_nodes(shell_keep(forces + with_base(shells), offset))

    rhs = rhs_wide[:, 2 : rows + 2, 2 : cols + 2]
    image_wide = node_keep(operate(rhs_wide, weights_wide, -2), -1)
    image = image_wide[:, 1 : rows + 1, 1 : cols + 1]
    again = operate(image_wide, weights_wide[:, 1 : rows + 2, 1 : cols + 2], -1)
    def lanes(values):
        values = jnp.stack(values)
        return jnp.broadcast_to(values[:, None], (values.shape[0], cols))

    first = all_sum(lanes([jnp.sum(rhs * rhs), jnp.sum(rhs * image)]))
    norm_now, curvature = first[0], first[1]
    alpha = norm_now / curvature
    residual = rhs - alpha * image
    bent = image - alpha * again
    second = all_sum(
        lanes(
            [
                jnp.sum(residual * residual),
                jnp.sum(residual * bent),
                jnp.sum(residual * image),
                jnp.sum(rhs * bent),
            ]
        )
    )
    norm_next = second[0]
    beta = norm_next / norm_now
    direction = residual + beta * rhs
    turned = bent + beta * image
    curvature_next = second[1] + beta * (second[2] + second[3]) + beta * beta * curvature
    alpha_next = norm_next / curvature_next
    solution = alpha * rhs + alpha_next * direction
    residual = residual - alpha_next * turned
    return (moved + solution, velocity_out, history_new.reshape(hist, rows, cols), residual)


def solution(mesh):
    return jax.shard_map(
        shards,
        mesh=mesh,
        in_specs=(
            P(None, "px", "py"),
            P(None, "px", "py"),
            P(None, "px", "py"),
            P(None, "px", "py"),
            P(None, "px", "py"),
            P(None, "px", "py"),
            P("px", "py", None, None),
            P(),
            P(),
            P("px", "py", None),
        ),
        out_specs=(
            P(None, "px", "py"),
            P(None, "px", "py"),
            P(None, "px", "py"),
            P(None, "px", "py"),
        ),
        check_vma=False,
    )
```

```python
import jax
import jax.numpy as jnp
from jax import lax
from jax.sharding import PartitionSpec as P

ITERS = 2


HIGH = lax.Precision.HIGHEST
STEP = 0.2
CORNERS = ((0, 0), (1, 0), (0, 1), (1, 1))


def with_halo(shard, before, after):
    for axis, dim in (("px", 1), ("py", 2)):
        devices, length = (lax.axis_size(axis), shard.shape[dim])
        up = [(i, i + 1) for i in range(devices - 1)]
        down = [(j, i) for i, j in up]
        parts = [shard]
        if before:
            last = lax.slice_in_dim(shard, length - before, length, axis=dim)
            parts.insert(0, lax.ppermute(last, axis, up))
        if after:
            leading = lax.slice_in_dim(shard, 0, after, axis=dim)
            parts.append(lax.ppermute(leading, axis, down))
        shard = jnp.concatenate(parts, axis=dim)
    return shard


def all_sum(value):
    for axis in ("px", "py"):
        devices = lax.axis_size(axis)
        stride = 1
        while stride < devices:
            radix = min(4, devices // stride)
            total = value
            for k in range(1, radix):
                pairs = []
                for i in range(devices):
                    digit = (i // stride) % radix
                    pairs.append((i, i + (((digit + k) % radix) - digit) * stride))
                total = total + lax.ppermute(value, axis, pairs)
            value = total
            stride *= radix
    return value


def gather_shells(field):
    rows, cols = (field.shape[1] - 1, field.shape[2] - 1)
    return jnp.concatenate(
        [field[:, dx : dx + rows, dy : dy + cols] for dx, dy in CORNERS], axis=0
    )


def scatter_nodes(forces):
    rows, cols = (forces.shape[1] - 1, forces.shape[2] - 1)
    total = jnp.zeros((6, rows, cols), jnp.float32)
    for index, (dx, dy) in enumerate(CORNERS):
        total = (
            total
            + forces[6 * index : 6 * index + 6, 1 - dx : 1 - dx + rows, 1 - dy : 1 - dy + cols]
        )
    return total


def inside(shape, row_from, col_from, rows_total, cols_total, low_only):
    rows, cols = shape
    row = lax.axis_index("px") * rows_total + row_from + jnp.arange(rows)
    col = lax.axis_index("py") * cols_total + col_from + jnp.arange(cols)
    row_ok = row >= 0
    col_ok = col >= 0
    if not low_only:
        row_ok = row_ok & (row < rows_total * lax.axis_size("px"))
        col_ok = col_ok & (col < cols_total * lax.axis_size("py"))
    return (row_ok[:, None] & col_ok[None, :]).astype(jnp.float32)


def shards(
    displacement,
    velocity,
    load,
    inv_mass,
    history,
    contact_home,
    recv_contact,
    stiff_base,
    strain_map,
    slot_table,
):
    hist = history.shape[0]
    rows, cols = (displacement.shape[1], displacement.shape[2])
    cells = rows * cols

    targets = slot_table.reshape(-1)
    devices = lax.axis_size("px") * lax.axis_size("py")
    width = targets.shape[0] // devices
    held = recv_contact.reshape(hist, devices, width).transpose(1, 2, 0).reshape(devices, -1)
    arrived = lax.all_to_all(held, ("px", "py"), split_axis=0, concat_axis=0, tiled=True)
    arrived = arrived.reshape(devices * width, hist).T

    def with_base(shells):
        return jnp.einsum("ab,bxy->axy", stiff_base, shells, precision=HIGH)

    def shell_keep(forces, offset):
        return forces * inside(forces.shape[1:], offset, offset, rows, cols, True)[None]

    def node_keep(field, offset):
        return field * inside(field.shape[1:], offset, offset, rows, cols, False)[None]

    both = with_halo(jnp.concatenate([displacement, load], axis=0), 3, 3)
    start_shells = gather_shells(both[:6])
    force_wide = scatter_nodes(shell_keep(with_base(start_shells), -3))
    force_start = force_wide[:, 2 : rows + 2, 2 : cols + 2]
    velocity_out = velocity + STEP * inv_mass * (load - force_start)
    moved = displacement + STEP * velocity_out
    own = start_shells[:, 3 : rows + 3, 3 : cols + 3].reshape(24, cells)
    history_new = history.reshape(hist, cells) + jnp.dot(strain_map, own, precision=HIGH)
    rhs_wide = node_keep(both[6:, 1 : rows + 5, 1 : cols + 5] - force_wide, -2)

    contact = (
        contact_home.reshape(hist, cells)
        .at[:, targets]
        .set(arrived, mode="drop")
    )
    weights = (jax.nn.softplus(history_new) * contact).reshape(hist, rows, cols)
    weights_wide = with_halo(weights, 2, 1)

    def operate(field, weights_of, offset):
        shells = gather_shells(field)
        strains = jnp.einsum("hb,bxy->hxy", strain_map, shells, precision=HIGH)
        forces = jnp.einsum("hb,hxy->bxy", strain_map, weights_of * strains, precision=HIGH)
        return scatter_nodes(shell_keep(forces + with_base(shells), offset))

    rhs = rhs_wide[:, 2 : rows + 2, 2 : cols + 2]
    image_wide = node_keep(operate(rhs_wide, weights_wide, -2), -1)
    image = image_wide[:, 1 : rows + 1, 1 : cols + 1]
    again = operate(image_wide, weights_wide[:, 1 : rows + 2, 1 : cols + 2], -1)
    def lanes(values):
        values = jnp.stack(values)
        return jnp.broadcast_to(values[:, None], (values.shape[0], cols))

    first = all_sum(lanes([jnp.sum(rhs * rhs), jnp.sum(rhs * image)]))
    norm_now, curvature = first[0], first[1]
    alpha = norm_now / curvature
    residual = rhs - alpha * image
    bent = image - alpha * again
    second = all_sum(
        lanes(
            [
                jnp.sum(residual * residual),
                jnp.sum(residual * bent),
                jnp.sum(residual * image),
                jnp.sum(rhs * bent),
            ]
        )
    )
    norm_next = second[0]
    beta = norm_next / norm_now
    direction = residual + beta * rhs
    turned = bent + beta * image
    curvature_next = second[1] + beta * (second[2] + second[3]) + beta * beta * curvature
    alpha_next = norm_next / curvature_next
    solution = alpha * rhs + alpha_next * direction
    residual = residual - alpha_next * turned
    return (moved + solution, velocity_out, history_new.reshape(hist, rows, cols), residual)


def solution(mesh):
    return jax.shard_map(
        shards,
        mesh=mesh,
        in_specs=(
            P(None, "px", "py"),
            P(None, "px", "py"),
            P(None, "px", "py"),
            P(None, "px", "py"),
            P(None, "px", "py"),
            P(None, "px", "py"),
            P("px", "py", None, None),
            P(),
            P(),
            P("px", "py", None),
        ),
        out_specs=(
            P(None, "px", "py"),
            P(None, "px", "py"),
            P(None, "px", "py"),
            P(None, "px", "py"),
        ),
        check_vma=False,
    )
```

```python
import jax
import jax.numpy as jnp
from jax import lax
from jax.sharding import PartitionSpec as P

ITERS = 2


HIGH = lax.Precision.HIGHEST
STEP = 0.2
CORNERS = ((0, 0), (1, 0), (0, 1), (1, 1))


def with_halo(shard, before, after):
    for axis, dim in (("px", 1), ("py", 2)):
        devices, length = (lax.axis_size(axis), shard.shape[dim])
        up = [(i, i + 1) for i in range(devices - 1)]
        down = [(j, i) for i, j in up]
        parts = [shard]
        if before:
            last = lax.slice_in_dim(shard, length - before, length, axis=dim)
            parts.insert(0, lax.ppermute(last, axis, up))
        if after:
            leading = lax.slice_in_dim(shard, 0, after, axis=dim)
            parts.append(lax.ppermute(leading, axis, down))
        shard = jnp.concatenate(parts, axis=dim)
    return shard


def all_sum(value):
    for axis in ("px", "py"):
        devices = lax.axis_size(axis)
        stride = 1
        while stride < devices:
            radix = min(4, devices // stride)
            total = value
            for k in range(1, radix):
                pairs = []
                for i in range(devices):
                    digit = (i // stride) % radix
                    pairs.append((i, i + (((digit + k) % radix) - digit) * stride))
                total = total + lax.ppermute(value, axis, pairs)
            value = total
            stride *= radix
    return value


def gather_shells(field):
    rows, cols = (field.shape[1] - 1, field.shape[2] - 1)
    return jnp.concatenate(
        [field[:, dx : dx + rows, dy : dy + cols] for dx, dy in CORNERS], axis=0
    )


def scatter_nodes(forces):
    rows, cols = (forces.shape[1] - 1, forces.shape[2] - 1)
    total = jnp.zeros((6, rows, cols), jnp.float32)
    for index, (dx, dy) in enumerate(CORNERS):
        total = (
            total
            + forces[6 * index : 6 * index + 6, 1 - dx : 1 - dx + rows, 1 - dy : 1 - dy + cols]
        )
    return total


def inside(shape, row_from, col_from, rows_total, cols_total, low_only):
    rows, cols = shape
    row = lax.axis_index("px") * rows_total + row_from + jnp.arange(rows)
    col = lax.axis_index("py") * cols_total + col_from + jnp.arange(cols)
    row_ok = row >= 0
    col_ok = col >= 0
    if not low_only:
        row_ok = row_ok & (row < rows_total * lax.axis_size("px"))
        col_ok = col_ok & (col < cols_total * lax.axis_size("py"))
    return (row_ok[:, None] & col_ok[None, :]).astype(jnp.float32)


def shards(
    displacement,
    velocity,
    load,
    inv_mass,
    history,
    contact_home,
    recv_contact,
    stiff_base,
    strain_map,
    slot_table,
):
    hist = history.shape[0]
    rows, cols = (displacement.shape[1], displacement.shape[2])
    cells = rows * cols

    targets = slot_table.reshape(-1)
    devices = lax.axis_size("px") * lax.axis_size("py")
    width = targets.shape[0] // devices
    held = recv_contact.reshape(hist, devices, width).transpose(1, 2, 0).reshape(devices, -1)
    arrived = lax.all_to_all(held, ("px", "py"), split_axis=0, concat_axis=0, tiled=True)
    arrived = arrived.reshape(devices * width, hist).T

    def with_base(shells):
        return jnp.einsum("ab,bxy->axy", stiff_base, shells, precision=HIGH)

    shell_mask = inside((rows + 5, cols + 5), -3, -3, rows, cols, True)
    node_mask = inside((rows + 4, cols + 4), -2, -2, rows, cols, False)

    def shell_keep(forces, offset):
        skip = offset + 3
        return forces * shell_mask[None, skip : skip + forces.shape[1], skip : skip + forces.shape[2]]

    def node_keep(field, offset):
        skip = offset + 2
        return field * node_mask[None, skip : skip + field.shape[1], skip : skip + field.shape[2]]

    both = with_halo(jnp.concatenate([displacement, load], axis=0), 3, 3)
    start_shells = gather_shells(both[:6])
    force_wide = scatter_nodes(shell_keep(with_base(start_shells), -3))
    force_start = force_wide[:, 2 : rows + 2, 2 : cols + 2]
    velocity_out = velocity + STEP * inv_mass * (load - force_start)
    moved = displacement + STEP * velocity_out
    own = start_shells[:, 3 : rows + 3, 3 : cols + 3].reshape(24, cells)
    history_new = history.reshape(hist, cells) + jnp.dot(strain_map, own, precision=HIGH)
    rhs_wide = node_keep(both[6:, 1 : rows + 5, 1 : cols + 5] - force_wide, -2)

    contact = (
        contact_home.reshape(hist, cells)
        .at[:, targets]
        .set(arrived, mode="drop")
    )
    weights = (jax.nn.softplus(history_new) * contact).reshape(hist, rows, cols)
    weights_wide = with_halo(weights, 2, 1)

    def operate(field, weights_of, offset):
        shells = gather_shells(field)
        strains = jnp.einsum("hb,bxy->hxy", strain_map, shells, precision=HIGH)
        forces = jnp.einsum("hb,hxy->bxy", strain_map, weights_of * strains, precision=HIGH)
        return scatter_nodes(shell_keep(forces + with_base(shells), offset))

    rhs = rhs_wide[:, 2 : rows + 2, 2 : cols + 2]
    image_wide = node_keep(operate(rhs_wide, weights_wide, -2), -1)
    image = image_wide[:, 1 : rows + 1, 1 : cols + 1]
    again = operate(image_wide, weights_wide[:, 1 : rows + 2, 1 : cols + 2], -1)
    def lanes(values):
        values = jnp.stack(values)
        return jnp.broadcast_to(values[:, None], (values.shape[0], cols))

    first = all_sum(lanes([jnp.sum(rhs * rhs), jnp.sum(rhs * image)]))
    norm_now, curvature = first[0], first[1]
    alpha = norm_now / curvature
    residual = rhs - alpha * image
    bent = image - alpha * again
    second = all_sum(
        lanes(
            [
                jnp.sum(residual * residual),
                jnp.sum(residual * bent),
                jnp.sum(residual * image),
                jnp.sum(rhs * bent),
            ]
        )
    )
    norm_next = second[0]
    beta = norm_next / norm_now
    direction = residual + beta * rhs
    turned = bent + beta * image
    curvature_next = second[1] + beta * (second[2] + second[3]) + beta * beta * curvature
    alpha_next = norm_next / curvature_next
    solution = alpha * rhs + alpha_next * direction
    residual = residual - alpha_next * turned
    return (moved + solution, velocity_out, history_new.reshape(hist, rows, cols), residual)


def solution(mesh):
    return jax.shard_map(
        shards,
        mesh=mesh,
        in_specs=(
            P(None, "px", "py"),
            P(None, "px", "py"),
            P(None, "px", "py"),
            P(None, "px", "py"),
            P(None, "px", "py"),
            P(None, "px", "py"),
            P("px", "py", None, None),
            P(),
            P(),
            P("px", "py", None),
        ),
        out_specs=(
            P(None, "px", "py"),
            P(None, "px", "py"),
            P(None, "px", "py"),
            P(None, "px", "py"),
        ),
        check_vma=False,
    )
```

```python
import jax
import jax.numpy as jnp
from jax import lax
from jax.sharding import PartitionSpec as P

ITERS = 2


HIGH = lax.Precision.HIGHEST
STEP = 0.2
CORNERS = ((0, 0), (1, 0), (0, 1), (1, 1))


def with_halo(shard, before, after):
    for axis, dim in (("px", 1), ("py", 2)):
        devices, length = (lax.axis_size(axis), shard.shape[dim])
        up = [(i, i + 1) for i in range(devices - 1)]
        down = [(j, i) for i, j in up]
        parts = [shard]
        if before:
            last = lax.slice_in_dim(shard, length - before, length, axis=dim)
            parts.insert(0, lax.ppermute(last, axis, up))
        if after:
            leading = lax.slice_in_dim(shard, 0, after, axis=dim)
            parts.append(lax.ppermute(leading, axis, down))
        shard = jnp.concatenate(parts, axis=dim)
    return shard


def all_sum(value):
    for axis in ("px", "py"):
        devices = lax.axis_size(axis)
        stride = 1
        while stride < devices:
            radix = min(4, devices // stride)
            total = value
            for k in range(1, radix):
                pairs = []
                for i in range(devices):
                    digit = (i // stride) % radix
                    pairs.append((i, i + (((digit + k) % radix) - digit) * stride))
                total = total + lax.ppermute(value, axis, pairs)
            value = total
            stride *= radix
    return value


def gather_shells(field):
    rows, cols = (field.shape[1] - 1, field.shape[2] - 1)
    return jnp.concatenate(
        [field[:, dx : dx + rows, dy : dy + cols] for dx, dy in CORNERS], axis=0
    )


def scatter_nodes(forces):
    rows, cols = (forces.shape[1] - 1, forces.shape[2] - 1)
    total = jnp.zeros((6, rows, cols), jnp.float32)
    for index, (dx, dy) in enumerate(CORNERS):
        total = (
            total
            + forces[6 * index : 6 * index + 6, 1 - dx : 1 - dx + rows, 1 - dy : 1 - dy + cols]
        )
    return total


def inside(shape, row_from, col_from, rows_total, cols_total, low_only):
    rows, cols = shape
    row = lax.axis_index("px") * rows_total + row_from + jnp.arange(rows)
    col = lax.axis_index("py") * cols_total + col_from + jnp.arange(cols)
    row_ok = row >= 0
    col_ok = col >= 0
    if not low_only:
        row_ok = row_ok & (row < rows_total * lax.axis_size("px"))
        col_ok = col_ok & (col < cols_total * lax.axis_size("py"))
    return (row_ok[:, None] & col_ok[None, :]).astype(jnp.float32)


def shards(
    displacement,
    velocity,
    load,
    inv_mass,
    history,
    contact_home,
    recv_contact,
    stiff_base,
    strain_map,
    slot_table,
):
    hist = history.shape[0]
    rows, cols = (displacement.shape[1], displacement.shape[2])
    cells = rows * cols

    targets = slot_table.reshape(-1)
    devices = lax.axis_size("px") * lax.axis_size("py")
    width = targets.shape[0] // devices
    held = recv_contact.reshape(hist, devices, width).transpose(1, 2, 0).reshape(devices, -1)
    arrived = lax.all_to_all(held, ("px", "py"), split_axis=0, concat_axis=0, tiled=True)
    arrived = arrived.reshape(devices * width, hist).T

    def with_base(shells):
        return jnp.einsum("ab,bxy->axy", stiff_base, shells, precision=HIGH)

    shell_mask = inside((rows + 5, cols + 5), -3, -3, rows, cols, True)
    node_mask = inside((rows + 4, cols + 4), -2, -2, rows, cols, False)

    def shell_keep(forces, offset):
        skip = offset + 3
        return forces * shell_mask[None, skip : skip + forces.shape[1], skip : skip + forces.shape[2]]

    def node_keep(field, offset):
        skip = offset + 2
        return field * node_mask[None, skip : skip + field.shape[1], skip : skip + field.shape[2]]

    both = with_halo(jnp.concatenate([displacement, load], axis=0), 3, 3)
    start_shells = gather_shells(both[:6])
    force_wide = scatter_nodes(shell_keep(with_base(start_shells), -3))
    force_start = force_wide[:, 2 : rows + 2, 2 : cols + 2]
    velocity_out = velocity + STEP * inv_mass * (load - force_start)
    moved = displacement + STEP * velocity_out
    own = start_shells[:, 3 : rows + 3, 3 : cols + 3].reshape(24, cells)
    history_new = history.reshape(hist, cells) + jnp.dot(strain_map, own, precision=HIGH)
    rhs_wide = node_keep(both[6:, 1 : rows + 5, 1 : cols + 5] - force_wide, -2)

    contact = (
        contact_home.reshape(hist, cells)
        .at[:, targets]
        .set(arrived, mode="drop")
    )
    weights = (jax.nn.softplus(history_new) * contact).reshape(hist, rows, cols)
    weights_wide = with_halo(weights, 2, 1)

    def operate(field, weights_of, offset):
        shells = gather_shells(field)
        strains = jnp.einsum("hb,bxy->hxy", strain_map, shells, precision=HIGH)
        forces = jnp.einsum("hb,hxy->bxy", strain_map, weights_of * strains, precision=HIGH)
        return scatter_nodes(shell_keep(forces + with_base(shells), offset))

    rhs = rhs_wide[:, 2 : rows + 2, 2 : cols + 2]
    image_wide = node_keep(operate(rhs_wide, weights_wide, -2), -1)
    image = image_wide[:, 1 : rows + 1, 1 : cols + 1]
    again = operate(image_wide, weights_wide[:, 1 : rows + 2, 1 : cols + 2], -1)
    def lanes(values):
        return jnp.stack([jnp.sum(value, axis=(0, 1)) for value in values])

    def totals(values):
        return jnp.broadcast_to(jnp.sum(values, axis=1, keepdims=True), values.shape)

    first = totals(all_sum(lanes([rhs * rhs, rhs * image])))
    norm_now, curvature = first[0], first[1]
    alpha = norm_now / curvature
    residual = rhs - alpha * image
    bent = image - alpha * again
    second = totals(
        all_sum(lanes([residual * residual, residual * bent, residual * image, rhs * bent]))
    )
    norm_next = second[0]
    beta = norm_next / norm_now
    direction = residual + beta * rhs
    turned = bent + beta * image
    curvature_next = second[1] + beta * (second[2] + second[3]) + beta * beta * curvature
    alpha_next = norm_next / curvature_next
    solution = alpha * rhs + alpha_next * direction
    residual = residual - alpha_next * turned
    return (moved + solution, velocity_out, history_new.reshape(hist, rows, cols), residual)


def solution(mesh):
    return jax.shard_map(
        shards,
        mesh=mesh,
        in_specs=(
            P(None, "px", "py"),
            P(None, "px", "py"),
            P(None, "px", "py"),
            P(None, "px", "py"),
            P(None, "px", "py"),
            P(None, "px", "py"),
            P("px", "py", None, None),
            P(),
            P(),
            P("px", "py", None),
        ),
        out_specs=(
            P(None, "px", "py"),
            P(None, "px", "py"),
            P(None, "px", "py"),
            P(None, "px", "py"),
        ),
        check_vma=False,
    )
```
